128 devices in a mesh: ctx: 16 (over x, z_lo, core), ch: 8 (over z_hi, y).
Axes of the slice: x: 4, y: 4, z: 4 (z_hi: 2, z_lo: 2; z = z_hi * 2 + z_lo), core: 2. Of those that a mesh axis runs over, the one named last changes fastest.
Arguments:
- q_proj: bfloat16 [16384, 4096], P(('ctx', 'ch')), may hold values from -6 to 6
- k_proj: bfloat16 [16384, 4096], P(('ctx', 'ch')), may hold values from -6 to 6
- v_proj: bfloat16 [16384, 4096], P(('ctx', 'ch')), may hold values from -6 to 6
- filter_taps: bfloat16 [16384, 4096], P(('ctx', 'ch')), may hold values from -6 to 6
- out_grad: bfloat16 [16384, 4096], P(('ctx', 'ch')), may hold values from -6 to 6
Outputs:
- mixed: bfloat16 [16384, 4096], P(('ctx', 'ch'))
- q_grad: bfloat16 [16384, 4096], P(('ctx', 'ch'))
- k_grad: bfloat16 [16384, 4096], P(('ctx', 'ch'))
- v_grad: bfloat16 [16384, 4096], P(('ctx', 'ch'))
- filter_grad: bfloat16 [16384, 4096], P(('ctx', 'ch'))
The draws below stay inside these ranges and needn't reach their ends.
All inputs are finite; a program needn't handle non-finite values.
Results may differ from the reference program's by a relative error of at most 0.013.
Values may be sent and summed in bfloat16 or wider, within the bound.
No kernel may reach another device: no remote copies, remote signals or barrier semaphores. Data moves between devices by JAX's collectives and lax.ppermute only.
A program may use at most 192 MiB of HBM per device.

```python
import math
import jax
import jax.numpy as jnp
from jax import lax

D = 4096
TOKENS = 16384


def levels(stream_key, dims, cuts, low, largest):
    def one(dim, blocks):
        heights = jax.random.uniform(jax.random.fold_in(jax.random.fold_in(stream_key, 6), dim), (blocks,), jnp.float32, low / len(cuts), largest / len(cuts))
        return jnp.repeat(jnp.exp(heights), dims[dim] // blocks).reshape((-1,) + (1,) * (len(dims) - dim - 1))

    factor_of = one(*cuts[0])
    for cut in cuts[1:]:
        factor_of = factor_of * one(*cut)
    return factor_of


def scatter_about(key, shape, deviation, bound, cuts=(), kind=jnp.bfloat16):
    values = jax.random.normal(key, shape, jnp.float32) * deviation
    if len(cuts) > 0:
        values = levels(key, shape, cuts, -0.22, 0.18) * values
    return jnp.clip(values, min=-bound, max=bound).astype(kind)


def setup_inputs(seed: int = 0) -> dict:
    splits = jax.random.split(jax.random.key(seed), 6)
    return {
        "q_proj": scatter_about(splits[0], (TOKENS, D), 1.0, 6.0, ((0, 128),)),
        "k_proj": scatter_about(splits[1], (TOKENS, D), 1.0, 6.0, ((0, 128),)),
        "v_proj": scatter_about(splits[2], (TOKENS, D), 1.0, 6.0, ((0, 128),)),
        "filter_taps": scatter_about(splits[3], (TOKENS, D), 1.0, 6.0, ((0, 128),)),
        "out_grad": scatter_about(splits[4], (TOKENS, D), 1.0, 6.0, ((0, 128),)),
    }


def reference(q_proj, k_proj, v_proj, filter_taps, out_grad):
    group = math.gcd(D, 256)
    padded = 2 * TOKENS
    norm_scale = 1.0 / math.sqrt(TOKENS)

    def split(array):
        return array.T.reshape(D // group, group, TOKENS)

    def one_group(pieces):
        queries = pieces[0].astype(jnp.float32)
        keys = pieces[1].astype(jnp.float32)
        values = pieces[2].astype(jnp.float32)
        taps = pieces[3].astype(jnp.float32)
        cotangent = pieces[4].astype(jnp.float32)
        gated = lax.optimization_barrier((keys * values).astype(jnp.bfloat16)).astype(jnp.float32)
        back_in = lax.optimization_barrier((cotangent * queries).astype(jnp.bfloat16)).astype(jnp.float32)
        taps_spec = jnp.fft.rfft(taps, padded, axis=-1)
        gated_spec = jnp.fft.rfft(gated, padded, axis=-1)
        back_spec = jnp.fft.rfft(back_in, padded, axis=-1)
        conv_out = norm_scale * jnp.fft.irfft(taps_spec * gated_spec, padded, axis=-1)[:, :TOKENS]
        conv_out = conv_out.astype(jnp.float32)
        mixed = (queries * conv_out).astype(jnp.bfloat16)
        q_grad = (cotangent * conv_out).astype(jnp.bfloat16)
        conv_grad = norm_scale * jnp.fft.irfft(jnp.conj(taps_spec) * back_spec, padded, axis=-1)[:, :TOKENS]
        conv_grad = conv_grad.astype(jnp.float32)
        k_grad = (conv_grad * values).astype(jnp.bfloat16)
        v_grad = (conv_grad * keys).astype(jnp.bfloat16)
        filter_grad = norm_scale * jnp.fft.irfft(back_spec * jnp.conj(gated_spec), padded, axis=-1)[:, :TOKENS]
        filter_grad = filter_grad.astype(jnp.float32).astype(jnp.bfloat16)
        return (mixed, q_grad, k_grad, v_grad, filter_grad)
    results = lax.map(one_group, (split(q_proj), split(k_proj), split(v_proj), split(filter_taps), split(out_grad)))
    mixed = results[0].reshape(D, TOKENS).T
    q_grad = results[1].reshape(D, TOKENS).T
    k_grad = results[2].reshape(D, TOKENS).T
    v_grad = results[3].reshape(D, TOKENS).T
    filter_grad = results[4].reshape(D, TOKENS).T
    return (mixed, q_grad, k_grad, v_grad, filter_grad)
```

```python
import math

import jax
import jax.numpy as jnp
from jax import lax
from jax.sharding import PartitionSpec as P

AXES = ("ctx", "ch")
F32 = jnp.float32
BF16 = jnp.bfloat16


def build_tables(first, second):
    points = first * second
    half = first // 2
    rows_first = jnp.arange(first, dtype=jnp.int32)
    rows_half = jnp.arange(half, dtype=jnp.int32)
    rows_second = jnp.arange(second, dtype=jnp.int32)
    outer_phase = rows_first[:, None] * rows_half[None, :] % first
    outer_angle = outer_phase.astype(F32) * (2.0 * math.pi / first)
    turn_phase = rows_first[:, None] * rows_second[None, :] % points
    turn_angle = turn_phase.astype(F32) * (2.0 * math.pi / points)
    inner_phase = rows_second[:, None] * rows_second[None, :] % second
    inner_angle = inner_phase.astype(F32) * (2.0 * math.pi / second)
    return (
        jnp.cos(outer_angle).astype(BF16),
        jnp.sin(outer_angle).astype(BF16),
        jnp.cos(turn_angle),
        jnp.sin(turn_angle),
        jnp.cos(inner_angle).astype(BF16),
        jnp.sin(inner_angle).astype(BF16),
    )


def mm(spec, left, right):
    return jnp.einsum(spec, left.astype(BF16), right.astype(BF16), preferred_element_type=F32)


def forward_spectrum(tables, signal):
    outer_cos, outer_sin, turn_cos, turn_sin, inner_cos, inner_sin = tables
    half = outer_cos.shape[1]
    second = inner_cos.shape[0]
    shaped = signal.reshape(signal.shape[0], half, second)
    real_outer = mm("kn,cnm->ckm", outer_cos, shaped)
    imag_outer = -mm("kn,cnm->ckm", outer_sin, shaped)
    real_turned = real_outer * turn_cos + imag_outer * turn_sin
    imag_turned = imag_outer * turn_cos - real_outer * turn_sin
    real_spec = mm("ckn,mn->ckm", real_turned, inner_cos) + mm("ckn,mn->ckm", imag_turned, inner_sin)
    imag_spec = mm("ckn,mn->ckm", imag_turned, inner_cos) - mm("ckn,mn->ckm", real_turned, inner_sin)
    return (real_spec, imag_spec)


def inverse_signal(tables, spec_pair, scale):
    outer_cos, outer_sin, turn_cos, turn_sin, inner_cos, inner_sin = tables
    real_spec, imag_spec = spec_pair
    real_inner = mm("ckn,mn->ckm", real_spec, inner_cos) - mm("ckn,mn->ckm", imag_spec, inner_sin)
    imag_inner = mm("ckn,mn->ckm", imag_spec, inner_cos) + mm("ckn,mn->ckm", real_spec, inner_sin)
    real_turned = (real_inner * turn_cos - imag_inner * turn_sin) * scale
    imag_turned = (imag_inner * turn_cos + real_inner * turn_sin) * scale
    result = mm("kn,ckm->cnm", outer_cos, real_turned) - mm("kn,ckm->cnm", outer_sin, imag_turned)
    return result.reshape(result.shape[0], -1)


def product(left_pair, right_pair):
    return (
        left_pair[0] * right_pair[0] - left_pair[1] * right_pair[1],
        left_pair[0] * right_pair[1] + left_pair[1] * right_pair[0],
    )


def product_conj(left_pair, right_pair):
    return (
        left_pair[0] * right_pair[0] + left_pair[1] * right_pair[1],
        left_pair[1] * right_pair[0] - left_pair[0] * right_pair[1],
    )


def to_channels(rows):
    return lax.all_to_all(jnp.swapaxes(rows, 1, 2), AXES, split_axis=1, concat_axis=2, tiled=True)


def to_tokens(cols):
    moved = lax.all_to_all(cols, AXES, split_axis=2, concat_axis=1, tiled=True)
    return jnp.swapaxes(moved, 1, 2)


def body(q_proj, k_proj, v_proj, filter_taps, out_grad):
    query = q_proj.astype(F32)
    key = k_proj.astype(F32)
    value = v_proj.astype(F32)
    cotangent = out_grad.astype(F32)
    gated = (key * value).astype(BF16)
    back_in = (cotangent * query).astype(BF16)

    forward_in = to_channels(jnp.stack([gated, filter_taps], 0))
    gated_part, taps_part = forward_in[0], forward_in[1]
    length = gated_part.shape[1]
    points = 2 * length
    second = math.gcd(points, 128)
    first = points // second
    tables = build_tables(first, second)
    scale = 1.0 / (math.sqrt(length) * points)

    gated_spec = forward_spectrum(tables, gated_part)
    taps_spec = forward_spectrum(tables, taps_part)
    conv_out = inverse_signal(tables, product(taps_spec, gated_spec), scale)
    conv_back = to_tokens(conv_out.astype(BF16)[None])[0].astype(F32)
    mixed = (query * conv_back).astype(BF16)
    q_grad = (cotangent * conv_back).astype(BF16)

    back_part = to_channels(back_in[None])[0]
    back_spec = forward_spectrum(tables, back_part)
    conv_grad = inverse_signal(tables, product_conj(back_spec, taps_spec), scale)
    filter_grad = inverse_signal(tables, product_conj(back_spec, gated_spec), scale)
    second_back = to_tokens(jnp.stack([conv_grad, filter_grad], 0).astype(BF16))
    grad_back = second_back[0].astype(F32)
    k_grad = (grad_back * value).astype(BF16)
    v_grad = (grad_back * key).astype(BF16)
    return (mixed, q_grad, k_grad, v_grad, second_back[1])


def solution(mesh):
    spec = P(AXES, None)
    return jax.shard_map(body, mesh=mesh, in_specs=(spec,) * 5, out_specs=(spec,) * 5, check_vma=False)
```

```python
import math

import jax
import jax.numpy as jnp
from jax import lax
from jax.sharding import PartitionSpec as P

AXES = ("ctx", "ch")
F32 = jnp.float32
BF16 = jnp.bfloat16


def build_tables(first, second):
    points = first * second
    half = first // 2
    rows_first = jnp.arange(first, dtype=jnp.int32)
    rows_half = jnp.arange(half, dtype=jnp.int32)
    rows_second = jnp.arange(second, dtype=jnp.int32)
    outer_phase = rows_first[:, None] * rows_half[None, :] % first
    outer_angle = outer_phase.astype(F32) * (2.0 * math.pi / first)
    turn_phase = rows_first[:, None] * rows_second[None, :] % points
    turn_angle = turn_phase.astype(F32) * (2.0 * math.pi / points)
    inner_phase = rows_second[:, None] * rows_second[None, :] % second
    inner_angle = inner_phase.astype(F32) * (2.0 * math.pi / second)
    return (
        jnp.cos(outer_angle).astype(BF16),
        jnp.sin(outer_angle).astype(BF16),
        jnp.cos(turn_angle),
        jnp.sin(turn_angle),
        jnp.cos(inner_angle).astype(BF16),
        jnp.sin(inner_angle).astype(BF16),
    )


def mm(spec, left, right):
    return jnp.einsum(spec, left.astype(BF16), right.astype(BF16), preferred_element_type=F32)


def forward_spectrum(tables, signal):
    outer_cos, outer_sin, turn_cos, turn_sin, inner_cos, inner_sin = tables
    half = outer_cos.shape[1]
    second = inner_cos.shape[0]
    shaped = signal.reshape(signal.shape[0], half, second)
    real_outer = mm("kn,cnm->ckm", outer_cos, shaped)
    imag_outer = -mm("kn,cnm->ckm", outer_sin, shaped)
    real_turned = real_outer * turn_cos + imag_outer * turn_sin
    imag_turned = imag_outer * turn_cos - real_outer * turn_sin
    real_spec = mm("ckn,mn->ckm", real_turned, inner_cos) + mm("ckn,mn->ckm", imag_turned, inner_sin)
    imag_spec = mm("ckn,mn->ckm", imag_turned, inner_cos) - mm("ckn,mn->ckm", real_turned, inner_sin)
    return (real_spec, imag_spec)


def inverse_signal(tables, spec_pair, scale):
    outer_cos, outer_sin, turn_cos, turn_sin, inner_cos, inner_sin = tables
    real_spec, imag_spec = spec_pair
    real_inner = mm("ckn,mn->ckm", real_spec, inner_cos) - mm("ckn,mn->ckm", imag_spec, inner_sin)
    imag_inner = mm("ckn,mn->ckm", imag_spec, inner_cos) + mm("ckn,mn->ckm", real_spec, inner_sin)
    real_turned = (real_inner * turn_cos - imag_inner * turn_sin) * scale
    imag_turned = (imag_inner * turn_cos + real_inner * turn_sin) * scale
    result = mm("kn,ckm->cnm", outer_cos, real_turned) - mm("kn,ckm->cnm", outer_sin, imag_turned)
    return result.reshape(result.shape[0], -1)


def product(left_pair, right_pair):
    return (
        left_pair[0] * right_pair[0] - left_pair[1] * right_pair[1],
        left_pair[0] * right_pair[1] + left_pair[1] * right_pair[0],
    )


def product_conj(left_pair, right_pair):
    return (
        left_pair[0] * right_pair[0] + left_pair[1] * right_pair[1],
        left_pair[1] * right_pair[0] - left_pair[0] * right_pair[1],
    )


def to_channels(arrays):
    rows, width = arrays[0].shape
    devices = lax.psum(1, AXES)
    per_device = width // devices
    packed = jnp.concatenate([a.T.reshape(devices, per_device, rows) for a in arrays], axis=1)
    moved = lax.all_to_all(packed, AXES, split_axis=0, concat_axis=0, tiled=True)
    moved = moved.reshape(devices, len(arrays), per_device, rows).transpose(1, 2, 0, 3)
    return moved.reshape(len(arrays), per_device, devices * rows)


def to_tokens(cols):
    count, per_device, length = cols.shape
    devices = lax.psum(1, AXES)
    rows = length // devices
    packed = cols.reshape(count, per_device, devices, rows).transpose(2, 0, 1, 3)
    moved = lax.all_to_all(packed.reshape(devices, count * per_device, rows), AXES, split_axis=0, concat_axis=0, tiled=True)
    moved = moved.reshape(devices, count, per_device, rows).transpose(1, 3, 0, 2)
    return moved.reshape(count, rows, devices * per_device)


def body(q_proj, k_proj, v_proj, filter_taps, out_grad):
    query = q_proj.astype(F32)
    key = k_proj.astype(F32)
    value = v_proj.astype(F32)
    cotangent = out_grad.astype(F32)
    gated = (key * value).astype(BF16)
    back_in = (cotangent * query).astype(BF16)

    forward_in = to_channels([gated, filter_taps])
    gated_part, taps_part = forward_in[0], forward_in[1]
    length = gated_part.shape[1]
    points = 2 * length
    second = math.gcd(points, 128)
    first = points // second
    tables = build_tables(first, second)
    scale = 1.0 / (math.sqrt(length) * points)

    gated_spec = forward_spectrum(tables, gated_part)
    taps_spec = forward_spectrum(tables, taps_part)
    conv_out = inverse_signal(tables, product(taps_spec, gated_spec), scale)
    conv_back = to_tokens(conv_out.astype(BF16).reshape((1,) + conv_out.shape))[0].astype(F32)
    mixed = (query * conv_back).astype(BF16)
    q_grad = (cotangent * conv_back).astype(BF16)

    back_part = to_channels([back_in])[0]
    back_spec = forward_spectrum(tables, back_part)
    conv_grad = inverse_signal(tables, product_conj(back_spec, taps_spec), scale)
    filter_grad = inverse_signal(tables, product_conj(back_spec, gated_spec), scale)
    second_back = to_tokens(jnp.stack([conv_grad, filter_grad], 0).astype(BF16))
    grad_back = second_back[0].astype(F32)
    k_grad = (grad_back * value).astype(BF16)
    v_grad = (grad_back * key).astype(BF16)
    return (mixed, q_grad, k_grad, v_grad, second_back[1])


def solution(mesh):
    spec = P(AXES, None)
    return jax.shard_map(body, mesh=mesh, in_specs=(spec,) * 5, out_specs=(spec,) * 5, check_vma=False)
```

```python
import math

import jax
import jax.numpy as jnp
from jax import lax
from jax.experimental import pallas as pl
from jax.experimental.pallas import tpu as pltpu
from jax.sharding import PartitionSpec as P

AXES = ("ctx", "ch")
F32 = jnp.float32
BF16 = jnp.bfloat16


def build_tables(first, second):
    points = first * second
    half = first // 2
    rows_first = jnp.arange(first, dtype=jnp.int32)
    rows_half = jnp.arange(half, dtype=jnp.int32)
    rows_second = jnp.arange(second, dtype=jnp.int32)
    outer_phase = rows_first[:, None] * rows_half[None, :] % first
    outer_angle = outer_phase.astype(F32) * (2.0 * math.pi / first)
    turn_phase = rows_first[:, None] * rows_second[None, :] % points
    turn_angle = turn_phase.astype(F32) * (2.0 * math.pi / points)
    inner_phase = rows_second[:, None] * rows_second[None, :] % second
    inner_angle = inner_phase.astype(F32) * (2.0 * math.pi / second)
    return (
        jnp.cos(outer_angle).astype(BF16),
        jnp.sin(outer_angle).astype(BF16),
        jnp.cos(turn_angle),
        jnp.sin(turn_angle),
        jnp.cos(inner_angle).astype(BF16),
        jnp.sin(inner_angle).astype(BF16),
    )


def mm(spec, left, right):
    return jnp.einsum(spec, left.astype(BF16), right.astype(BF16), preferred_element_type=F32)


def forward_spectrum(tables, signal):
    outer_cos, outer_sin, turn_cos, turn_sin, inner_cos, inner_sin = tables
    half = outer_cos.shape[1]
    second = inner_cos.shape[0]
    shaped = signal.reshape(signal.shape[0], half, second)
    real_outer = mm("kn,cnm->ckm", outer_cos, shaped)
    imag_outer = -mm("kn,cnm->ckm", outer_sin, shaped)
    real_turned = real_outer * turn_cos + imag_outer * turn_sin
    imag_turned = imag_outer * turn_cos - real_outer * turn_sin
    real_spec = mm("ckn,mn->ckm", real_turned, inner_cos) + mm("ckn,mn->ckm", imag_turned, inner_sin)
    imag_spec = mm("ckn,mn->ckm", imag_turned, inner_cos) - mm("ckn,mn->ckm", real_turned, inner_sin)
    return (real_spec, imag_spec)


def inverse_signal(tables, spec_pair, scale):
    outer_cos, outer_sin, turn_cos, turn_sin, inner_cos, inner_sin = tables
    real_spec, imag_spec = spec_pair
    real_inner = mm("ckn,mn->ckm", real_spec, inner_cos) - mm("ckn,mn->ckm", imag_spec, inner_sin)
    imag_inner = mm("ckn,mn->ckm", imag_spec, inner_cos) + mm("ckn,mn->ckm", real_spec, inner_sin)
    real_turned = (real_inner * turn_cos - imag_inner * turn_sin) * scale
    imag_turned = (imag_inner * turn_cos + real_inner * turn_sin) * scale
    result = mm("kn,ckm->cnm", outer_cos, real_turned) - mm("kn,ckm->cnm", outer_sin, imag_turned)
    return result.reshape(result.shape[0], -1)


def product(left_pair, right_pair):
    return (
        left_pair[0] * right_pair[0] - left_pair[1] * right_pair[1],
        left_pair[0] * right_pair[1] + left_pair[1] * right_pair[0],
    )


def product_conj(left_pair, right_pair):
    return (
        left_pair[0] * right_pair[0] + left_pair[1] * right_pair[1],
        left_pair[1] * right_pair[0] - left_pair[0] * right_pair[1],
    )


def to_channels(arrays):
    rows, width = arrays[0].shape
    devices = lax.psum(1, AXES)
    per_device = width // devices
    packed = jnp.concatenate([a.T.reshape(devices, per_device, rows) for a in arrays], axis=1)
    moved = lax.all_to_all(packed, AXES, split_axis=0, concat_axis=0, tiled=True)
    moved = moved.reshape(devices, len(arrays), per_device, rows).transpose(1, 2, 0, 3)
    return moved.reshape(len(arrays), per_device, devices * rows)


def to_tokens(cols):
    count, per_device, length = cols.shape
    devices = lax.psum(1, AXES)
    rows = length // devices
    packed = cols.reshape(count, per_device, devices, rows).transpose(2, 0, 1, 3)
    moved = lax.all_to_all(packed.reshape(devices, count * per_device, rows), AXES, split_axis=0, concat_axis=0, tiled=True)
    moved = moved.reshape(devices, count, per_device, rows).transpose(1, 3, 0, 2)
    return moved.reshape(count, rows, devices * per_device)


def kernel_tables(first, second):
    outer_cos, outer_sin, turn_cos, turn_sin, inner_cos, inner_sin = build_tables(first, second)
    stage_one = jnp.concatenate([outer_cos, -outer_sin], axis=0)
    forward_two = jnp.concatenate(
        [jnp.concatenate([inner_cos, -inner_sin], axis=1), jnp.concatenate([inner_sin, inner_cos], axis=1)], axis=0
    )
    inverse_two = jnp.concatenate(
        [jnp.concatenate([inner_cos, inner_sin], axis=1), jnp.concatenate([-inner_sin, inner_cos], axis=1)], axis=0
    )
    stage_last = jnp.concatenate([outer_cos.T, -outer_sin.T], axis=1)
    return (stage_one, turn_cos, turn_sin, forward_two, inverse_two, stage_last)


def conv_kernel(scale, block, fwd_ref, back_ref, one_ref, tc_ref, ts_ref, two_ref, inv_ref, last_ref, out_ref):
    first = tc_ref.shape[0]
    second = tc_ref.shape[1]

    def dot(left, right):
        return jnp.dot(left, right, preferred_element_type=F32)

    def spectrum(signal):
        outer = dot(one_ref[...], signal)
        real, imag = outer[:first], outer[first:]
        turn_c, turn_s = tc_ref[...], ts_ref[...]
        turned = jnp.concatenate([real * turn_c + imag * turn_s, imag * turn_c - real * turn_s], axis=1)
        spec = dot(turned.astype(BF16), two_ref[...])
        return spec[:, :second], spec[:, second:]

    def inverse(real, imag):
        inner = dot(jnp.concatenate([real, imag], axis=1).astype(BF16), inv_ref[...])
        inner_re, inner_im = inner[:, :second], inner[:, second:]
        turn_c, turn_s = tc_ref[...] * scale, ts_ref[...] * scale
        turned = jnp.concatenate([inner_re * turn_c - inner_im * turn_s, inner_im * turn_c + inner_re * turn_s], axis=0)
        return dot(last_ref[...], turned.astype(BF16))

    def one_channel(c, carry):
        g_re, g_im = spectrum(fwd_ref[0, c])
        t_re, t_im = spectrum(fwd_ref[1, c])
        out_ref[0, c] = inverse(t_re * g_re - t_im * g_im, t_re * g_im + t_im * g_re).astype(out_ref.dtype)
        b_re, b_im = spectrum(back_ref[0, c])
        out_ref[1, c] = inverse(b_re * t_re + b_im * t_im, b_im * t_re - b_re * t_im).astype(out_ref.dtype)
        out_ref[2, c] = inverse(b_re * g_re + b_im * g_im, b_im * g_re - b_re * g_im).astype(out_ref.dtype)
        return carry

    lax.fori_loop(0, block, one_channel, 0)


def convolve(forward_in, back_part, block=4):
    _, channels, length = forward_in.shape
    points = 2 * length
    second = math.gcd(points, 128)
    first = points // second
    half = first // 2
    tables = kernel_tables(first, second)
    scale = 1.0 / (math.sqrt(length) * points)
    fwd = forward_in.reshape(2, channels, half, second)
    back = back_part.reshape(1, channels, half, second)

    def whole(shape):
        return pl.BlockSpec(shape, lambda i: (0,) * len(shape))

    out = pl.pallas_call(
        lambda *refs: conv_kernel(scale, block, *refs),
        grid=(channels // block,),
        in_specs=[
            pl.BlockSpec((2, block, half, second), lambda i: (0, i, 0, 0)),
            pl.BlockSpec((1, block, half, second), lambda i: (0, i, 0, 0)),
        ]
        + [whole(t.shape) for t in tables],
        out_specs=pl.BlockSpec((3, block, half, second), lambda i: (0, i, 0, 0)),
        out_shape=jax.ShapeDtypeStruct((3, channels, half, second), BF16),
        compiler_params=pltpu.CompilerParams(dimension_semantics=("arbitrary",)),
        name="hyena_conv",
    )(fwd, back, *tables)
    return out.reshape(3, channels, length)


def body(q_proj, k_proj, v_proj, filter_taps, out_grad):
    query = q_proj.astype(F32)
    key = k_proj.astype(F32)
    value = v_proj.astype(F32)
    cotangent = out_grad.astype(F32)
    gated = (key * value).astype(BF16)
    back_in = (cotangent * query).astype(BF16)

    forward_in = to_channels([gated, filter_taps])
    back_part = to_channels([back_in])
    results = convolve(forward_in, back_part)
    moved = to_tokens(results)
    conv_back = moved[0].astype(F32)
    grad_back = moved[1].astype(F32)
    mixed = (query * conv_back).astype(BF16)
    q_grad = (cotangent * conv_back).astype(BF16)
    k_grad = (grad_back * value).astype(BF16)
    v_grad = (grad_back * key).astype(BF16)
    return (mixed, q_grad, k_grad, v_grad, moved[2])


def solution(mesh):
    spec = P(AXES, None)
    return jax.shard_map(body, mesh=mesh, in_specs=(spec,) * 5, out_specs=(spec,) * 5, check_vma=False)
```

```python
import math

import jax
import jax.numpy as jnp
from jax import lax
from jax.experimental import pallas as pl
from jax.experimental.pallas import tpu as pltpu
from jax.sharding import PartitionSpec as P

AXES = ("ctx", "ch")
F32 = jnp.float32
BF16 = jnp.bfloat16


def build_tables(first, second):
    points = first * second
    half = first // 2
    rows_first = jnp.arange(first, dtype=jnp.int32)
    rows_half = jnp.arange(half, dtype=jnp.int32)
    rows_second = jnp.arange(second, dtype=jnp.int32)
    outer_phase = rows_first[:, None] * rows_half[None, :] % first
    outer_angle = outer_phase.astype(F32) * (2.0 * math.pi / first)
    turn_phase = rows_first[:, None] * rows_second[None, :] % points
    turn_angle = turn_phase.astype(F32) * (2.0 * math.pi / points)
    inner_phase = rows_second[:, None] * rows_second[None, :] % second
    inner_angle = inner_phase.astype(F32) * (2.0 * math.pi / second)
    return (
        jnp.cos(outer_angle).astype(BF16),
        jnp.sin(outer_angle).astype(BF16),
        jnp.cos(turn_angle),
        jnp.sin(turn_angle),
        jnp.cos(inner_angle).astype(BF16),
        jnp.sin(inner_angle).astype(BF16),
    )


def mm(spec, left, right):
    return jnp.einsum(spec, left.astype(BF16), right.astype(BF16), preferred_element_type=F32)


def forward_spectrum(tables, signal):
    outer_cos, outer_sin, turn_cos, turn_sin, inner_cos, inner_sin = tables
    half = outer_cos.shape[1]
    second = inner_cos.shape[0]
    shaped = signal.reshape(signal.shape[0], half, second)
    real_outer = mm("kn,cnm->ckm", outer_cos, shaped)
    imag_outer = -mm("kn,cnm->ckm", outer_sin, shaped)
    real_turned = real_outer * turn_cos + imag_outer * turn_sin
    imag_turned = imag_outer * turn_cos - real_outer * turn_sin
    real_spec = mm("ckn,mn->ckm", real_turned, inner_cos) + mm("ckn,mn->ckm", imag_turned, inner_sin)
    imag_spec = mm("ckn,mn->ckm", imag_turned, inner_cos) - mm("ckn,mn->ckm", real_turned, inner_sin)
    return (real_spec, imag_spec)


def inverse_signal(tables, spec_pair, scale):
    outer_cos, outer_sin, turn_cos, turn_sin, inner_cos, inner_sin = tables
    real_spec, imag_spec = spec_pair
    real_inner = mm("ckn,mn->ckm", real_spec, inner_cos) - mm("ckn,mn->ckm", imag_spec, inner_sin)
    imag_inner = mm("ckn,mn->ckm", imag_spec, inner_cos) + mm("ckn,mn->ckm", real_spec, inner_sin)
    real_turned = (real_inner * turn_cos - imag_inner * turn_sin) * scale
    imag_turned = (imag_inner * turn_cos + real_inner * turn_sin) * scale
    result = mm("kn,ckm->cnm", outer_cos, real_turned) - mm("kn,ckm->cnm", outer_sin, imag_turned)
    return result.reshape(result.shape[0], -1)


def product(left_pair, right_pair):
    return (
        left_pair[0] * right_pair[0] - left_pair[1] * right_pair[1],
        left_pair[0] * right_pair[1] + left_pair[1] * right_pair[0],
    )


def product_conj(left_pair, right_pair):
    return (
        left_pair[0] * right_pair[0] + left_pair[1] * right_pair[1],
        left_pair[1] * right_pair[0] - left_pair[0] * right_pair[1],
    )


def to_channels(arrays):
    rows, width = arrays[0].shape
    devices = lax.psum(1, AXES)
    per_device = width // devices
    packed = jnp.concatenate([a.T.reshape(devices, per_device, rows) for a in arrays], axis=1)
    moved = lax.all_to_all(packed, AXES, split_axis=0, concat_axis=0, tiled=True)
    moved = moved.reshape(devices, len(arrays), per_device, rows).transpose(1, 2, 0, 3)
    return moved.reshape(len(arrays), per_device, devices * rows)


def to_tokens(cols):
    count, per_device, length = cols.shape
    devices = lax.psum(1, AXES)
    rows = length // devices
    packed = cols.reshape(count, per_device, devices, rows).transpose(2, 0, 1, 3)
    moved = lax.all_to_all(packed.reshape(devices, count * per_device, rows), AXES, split_axis=0, concat_axis=0, tiled=True)
    moved = moved.reshape(devices, count, per_device, rows).transpose(1, 3, 0, 2)
    return moved.reshape(count, rows, devices * per_device)


def kernel_tables(first, second):
    outer_cos, outer_sin, turn_cos, turn_sin, inner_cos, inner_sin = build_tables(first, second)
    stage_one = jnp.concatenate([outer_cos, -outer_sin], axis=0)
    forward_two = jnp.concatenate(
        [jnp.concatenate([inner_cos, -inner_sin], axis=1), jnp.concatenate([inner_sin, inner_cos], axis=1)], axis=0
    )
    inverse_two = jnp.concatenate(
        [jnp.concatenate([inner_cos, inner_sin], axis=1), jnp.concatenate([-inner_sin, inner_cos], axis=1)], axis=0
    )
    stage_last = jnp.concatenate([outer_cos.T, -outer_sin.T], axis=1)
    return (stage_one, turn_cos, turn_sin, forward_two, inverse_two, stage_last)


def conv_kernel(scale, block, fwd_ref, back_ref, one_ref, tc_ref, ts_ref, two_ref, inv_ref, last_ref, out_ref):
    first = tc_ref.shape[0]
    second = tc_ref.shape[1]

    def dot(left, right):
        return jnp.dot(left, right, preferred_element_type=F32)

    def spectrum(signal):
        outer = dot(one_ref[...], signal)
        real, imag = outer[:first], outer[first:]
        turn_c, turn_s = tc_ref[...], ts_ref[...]
        turned = jnp.concatenate([real * turn_c + imag * turn_s, imag * turn_c - real * turn_s], axis=1)
        spec = dot(turned.astype(BF16), two_ref[...])
        return spec[:, :second], spec[:, second:]

    def inverse(real, imag):
        inner = dot(jnp.concatenate([real, imag], axis=1).astype(BF16), inv_ref[...])
        inner_re, inner_im = inner[:, :second], inner[:, second:]
        turn_c, turn_s = tc_ref[...] * scale, ts_ref[...] * scale
        turned = jnp.concatenate([inner_re * turn_c - inner_im * turn_s, inner_im * turn_c + inner_re * turn_s], axis=0)
        return dot(last_ref[...], turned.astype(BF16))

    def one_channel(c, carry):
        g_re, g_im = spectrum(fwd_ref[0, c])
        t_re, t_im = spectrum(fwd_ref[1, c])
        out_ref[0, c] = inverse(t_re * g_re - t_im * g_im, t_re * g_im + t_im * g_re).astype(out_ref.dtype)
        b_re, b_im = spectrum(back_ref[0, c])
        out_ref[1, c] = inverse(b_re * t_re + b_im * t_im, b_im * t_re - b_re * t_im).astype(out_ref.dtype)
        out_ref[2, c] = inverse(b_re * g_re + b_im * g_im, b_im * g_re - b_re * g_im).astype(out_ref.dtype)
        return carry

    lax.fori_loop(0, block, one_channel, 0)


def convolve(forward_in, back_part, block=4):
    _, channels, length = forward_in.shape
    points = 2 * length
    second = math.gcd(points, 128)
    first = points // second
    half = first // 2
    tables = kernel_tables(first, second)
    scale = 1.0 / (math.sqrt(length) * points)
    fwd = forward_in.reshape(2, channels, half, second)
    back = back_part.reshape(1, channels, half, second)

    def whole(shape):
        return pl.BlockSpec(shape, lambda i: (0,) * len(shape))

    out = pl.pallas_call(
        lambda *refs: conv_kernel(scale, block, *refs),
        grid=(channels // block,),
        in_specs=[
            pl.BlockSpec((2, block, half, second), lambda i: (0, i, 0, 0)),
            pl.BlockSpec((1, block, half, second), lambda i: (0, i, 0, 0)),
        ]
        + [whole(t.shape) for t in tables],
        out_specs=pl.BlockSpec((3, block, half, second), lambda i: (0, i, 0, 0)),
        out_shape=jax.ShapeDtypeStruct((3, channels, half, second), BF16),
        compiler_params=pltpu.CompilerParams(dimension_semantics=("arbitrary",)),
        name="hyena_conv",
    )(fwd, back, *tables)
    return out.reshape(3, channels, length)


def body(q_proj, k_proj, v_proj, filter_taps, out_grad, chunks=2):
    query = q_proj.astype(F32)
    key = k_proj.astype(F32)
    value = v_proj.astype(F32)
    cotangent = out_grad.astype(F32)
    gated = (key * value).astype(BF16)
    back_in = (cotangent * query).astype(BF16)

    width = gated.shape[1] // chunks
    inputs = [
        to_channels([a[:, h * width:(h + 1) * width] for a in (gated, filter_taps, back_in)]) for h in range(chunks)
    ]
    pieces = [to_tokens(convolve(part[:2], part[2:])) for part in inputs]
    moved = jnp.concatenate(pieces, axis=2)
    conv_back = moved[0].astype(F32)
    grad_back = moved[1].astype(F32)
    mixed = (query * conv_back).astype(BF16)
    q_grad = (cotangent * conv_back).astype(BF16)
    k_grad = (grad_back * value).astype(BF16)
    v_grad = (grad_back * key).astype(BF16)
    return (mixed, q_grad, k_grad, v_grad, moved[2])


def solution(mesh):
    spec = P(AXES, None)
    return jax.shard_map(body, mesh=mesh, in_specs=(spec,) * 5, out_specs=(spec,) * 5, check_vma=False)
```

```python
import math

import jax
import jax.numpy as jnp
from jax import lax
from jax.experimental import pallas as pl
from jax.experimental.pallas import tpu as pltpu
from jax.sharding import PartitionSpec as P

AXES = ("ctx", "ch")
F32 = jnp.float32
BF16 = jnp.bfloat16


def build_tables(first, second):
    points = first * second
    half = first // 2
    rows_first = jnp.arange(first, dtype=jnp.int32)
    rows_half = jnp.arange(half, dtype=jnp.int32)
    rows_second = jnp.arange(second, dtype=jnp.int32)
    outer_phase = rows_first[:, None] * rows_half[None, :] % first
    outer_angle = outer_phase.astype(F32) * (2.0 * math.pi / first)
    turn_phase = rows_first[:, None] * rows_second[None, :] % points
    turn_angle = turn_phase.astype(F32) * (2.0 * math.pi / points)
    inner_phase = rows_second[:, None] * rows_second[None, :] % second
    inner_angle = inner_phase.astype(F32) * (2.0 * math.pi / second)
    return (
        jnp.cos(outer_angle).astype(BF16),
        jnp.sin(outer_angle).astype(BF16),
        jnp.cos(turn_angle),
        jnp.sin(turn_angle),
        jnp.cos(inner_angle).astype(BF16),
        jnp.sin(inner_angle).astype(BF16),
    )


def mm(spec, left, right):
    return jnp.einsum(spec, left.astype(BF16), right.astype(BF16), preferred_element_type=F32)


def forward_spectrum(tables, signal):
    outer_cos, outer_sin, turn_cos, turn_sin, inner_cos, inner_sin = tables
    half = outer_cos.shape[1]
    second = inner_cos.shape[0]
    shaped = signal.reshape(signal.shape[0], half, second)
    real_outer = mm("kn,cnm->ckm", outer_cos, shaped)
    imag_outer = -mm("kn,cnm->ckm", outer_sin, shaped)
    real_turned = real_outer * turn_cos + imag_outer * turn_sin
    imag_turned = imag_outer * turn_cos - real_outer * turn_sin
    real_spec = mm("ckn,mn->ckm", real_turned, inner_cos) + mm("ckn,mn->ckm", imag_turned, inner_sin)
    imag_spec = mm("ckn,mn->ckm", imag_turned, inner_cos) - mm("ckn,mn->ckm", real_turned, inner_sin)
    return (real_spec, imag_spec)


def inverse_signal(tables, spec_pair, scale):
    outer_cos, outer_sin, turn_cos, turn_sin, inner_cos, inner_sin = tables
    real_spec, imag_spec = spec_pair
    real_inner = mm("ckn,mn->ckm", real_spec, inner_cos) - mm("ckn,mn->ckm", imag_spec, inner_sin)
    imag_inner = mm("ckn,mn->ckm", imag_spec, inner_cos) + mm("ckn,mn->ckm", real_spec, inner_sin)
    real_turned = (real_inner * turn_cos - imag_inner * turn_sin) * scale
    imag_turned = (imag_inner * turn_cos + real_inner * turn_sin) * scale
    result = mm("kn,ckm->cnm", outer_cos, real_turned) - mm("kn,ckm->cnm", outer_sin, imag_turned)
    return result.reshape(result.shape[0], -1)


def product(left_pair, right_pair):
    return (
        left_pair[0] * right_pair[0] - left_pair[1] * right_pair[1],
        left_pair[0] * right_pair[1] + left_pair[1] * right_pair[0],
    )


def product_conj(left_pair, right_pair):
    return (
        left_pair[0] * right_pair[0] + left_pair[1] * right_pair[1],
        left_pair[1] * right_pair[0] - left_pair[0] * right_pair[1],
    )


def to_channels(arrays):
    rows, width = arrays[0].shape
    devices = lax.psum(1, AXES)
    per_device = width // devices
    packed = jnp.concatenate([a.T.reshape(devices, per_device, rows) for a in arrays], axis=1)
    moved = lax.all_to_all(packed, AXES, split_axis=0, concat_axis=0, tiled=True)
    moved = moved.reshape(devices, len(arrays), per_device, rows).transpose(1, 2, 0, 3)
    return moved.reshape(len(arrays), per_device, devices * rows)


def to_tokens(cols):
    count, per_device, length = cols.shape
    devices = lax.psum(1, AXES)
    rows = length // devices
    packed = cols.reshape(count, per_device, devices, rows).transpose(2, 0, 1, 3)
    moved = lax.all_to_all(packed.reshape(devices, count * per_device, rows), AXES, split_axis=0, concat_axis=0, tiled=True)
    moved = moved.reshape(devices, count, per_device, rows).transpose(1, 3, 0, 2)
    return moved.reshape(count, rows, devices * per_device)


def kernel_tables(first, second, rows):
    outer_cos, outer_sin, turn_cos, turn_sin, inner_cos, inner_sin = build_tables(first, second)
    stage_one = jnp.concatenate([outer_cos[:rows], -outer_sin[:rows]], axis=0)
    forward_two = jnp.concatenate(
        [jnp.concatenate([inner_cos, -inner_sin], axis=1), jnp.concatenate([inner_sin, inner_cos], axis=1)], axis=0
    )
    inverse_two = jnp.concatenate(
        [jnp.concatenate([inner_cos, inner_sin], axis=1), jnp.concatenate([-inner_sin, inner_cos], axis=1)], axis=0
    )
    index = jnp.arange(rows)
    weight = jnp.where((index == 0) | (index == first // 2), 1.0, jnp.where(index < first // 2, 2.0, 0.0))
    weight = weight.astype(F32)[None, :]
    stage_last = jnp.concatenate(
        [outer_cos[:rows].T.astype(F32) * weight, -outer_sin[:rows].T.astype(F32) * weight], axis=1
    )
    return (stage_one, turn_cos[:rows], turn_sin[:rows], forward_two, inverse_two, stage_last)


def conv_kernel(block, fwd_ref, back_ref, one_ref, tc_ref, ts_ref, two_ref, inv_ref, last_ref, out_ref, turned_ref, spec_ref):
    first = tc_ref.shape[0]
    second = tc_ref.shape[1]

    def dot(left, right):
        return jnp.dot(left, right, preferred_element_type=F32)

    def rows_of(signal, c):
        return pl.ds(pl.multiple_of((signal * block + c) * first, first), first)

    def stage_one(c, carry):
        for signal, source in enumerate((fwd_ref.at[0], fwd_ref.at[1], back_ref.at[0])):
            outer = dot(one_ref[...], source[c])
            real, imag = outer[:first], outer[first:]
            turn_c, turn_s = tc_ref[...], ts_ref[...]
            turned = jnp.concatenate([real * turn_c + imag * turn_s, imag * turn_c - real * turn_s], axis=1)
            turned_ref[rows_of(signal, c), :] = turned.astype(BF16)
        return carry

    lax.fori_loop(0, block, stage_one, 0)
    spec_ref[...] = dot(turned_ref[...], two_ref[...])

    def products(c, carry):
        g = spec_ref[rows_of(0, c), :]
        t = spec_ref[rows_of(1, c), :]
        b = spec_ref[rows_of(2, c), :]
        g_re, g_im = g[:, :second], g[:, second:]
        t_re, t_im = t[:, :second], t[:, second:]
        b_re, b_im = b[:, :second], b[:, second:]
        pairs = (
            (t_re * g_re - t_im * g_im, t_re * g_im + t_im * g_re),
            (b_re * t_re + b_im * t_im, b_im * t_re - b_re * t_im),
            (b_re * g_re + b_im * g_im, b_im * g_re - b_re * g_im),
        )
        for j, (real, imag) in enumerate(pairs):
            turned_ref[rows_of(j, c), :] = jnp.concatenate([real, imag], axis=1).astype(BF16)
        return carry

    lax.fori_loop(0, block, products, 0)
    spec_ref[...] = dot(turned_ref[...], inv_ref[...])

    def stage_last(c, carry):
        turn_c, turn_s = tc_ref[...], ts_ref[...]
        for j in range(3):
            inner = spec_ref[rows_of(j, c), :]
            inner_re, inner_im = inner[:, :second], inner[:, second:]
            turned = jnp.concatenate(
                [inner_re * turn_c - inner_im * turn_s, inner_im * turn_c + inner_re * turn_s], axis=0
            )
            out_ref[j, c] = dot(last_ref[...], turned.astype(BF16)).astype(out_ref.dtype)
        return carry

    lax.fori_loop(0, block, stage_last, 0)


def convolve(forward_in, back_part, block=8, rows=144):
    _, channels, length = forward_in.shape
    points = 2 * length
    second = math.gcd(points, 128)
    first = points // second
    half = first // 2
    scale = 1.0 / (math.sqrt(length) * points)
    stage_one, turn_c, turn_s, forward_two, inverse_two, stage_last = kernel_tables(first, second, rows)
    tables = (stage_one, turn_c, turn_s, forward_two, inverse_two, (stage_last.astype(F32) * scale).astype(BF16))
    fwd = forward_in.reshape(2, channels, half, second)
    back = back_part.reshape(1, channels, half, second)

    def whole(shape):
        return pl.BlockSpec(shape, lambda i: (0,) * len(shape))

    out = pl.pallas_call(
        lambda *refs: conv_kernel(block, *refs),
        grid=(channels // block,),
        in_specs=[
            pl.BlockSpec((2, block, half, second), lambda i: (0, i, 0, 0)),
            pl.BlockSpec((1, block, half, second), lambda i: (0, i, 0, 0)),
        ]
        + [whole(t.shape) for t in tables],
        out_specs=pl.BlockSpec((3, block, half, second), lambda i: (0, i, 0, 0)),
        out_shape=jax.ShapeDtypeStruct((3, channels, half, second), BF16),
        scratch_shapes=[pltpu.VMEM((3 * block * rows, 2 * second), BF16), pltpu.VMEM((3 * block * rows, 2 * second), F32)],
        compiler_params=pltpu.CompilerParams(dimension_semantics=("arbitrary",)),
        name="hyena_conv",
    )(fwd, back, *tables)
    return out.reshape(3, channels, length)


def body(q_proj, k_proj, v_proj, filter_taps, out_grad, chunks=2):
    query = q_proj.astype(F32)
    key = k_proj.astype(F32)
    value = v_proj.astype(F32)
    cotangent = out_grad.astype(F32)
    gated = (key * value).astype(BF16)
    back_in = (cotangent * query).astype(BF16)

    width = gated.shape[1] // chunks
    inputs = [
        to_channels([a[:, h * width:(h + 1) * width] for a in (gated, filter_taps, back_in)]) for h in range(chunks)
    ]
    pieces = [to_tokens(convolve(part[:2], part[2:])) for part in inputs]
    moved = jnp.concatenate(pieces, axis=2)
    conv_back = moved[0].astype(F32)
    grad_back = moved[1].astype(F32)
    mixed = (query * conv_back).astype(BF16)
    q_grad = (cotangent * conv_back).astype(BF16)
    k_grad = (grad_back * value).astype(BF16)
    v_grad = (grad_back * key).astype(BF16)
    return (mixed, q_grad, k_grad, v_grad, moved[2])


def solution(mesh):
    spec = P(AXES, None)
    return jax.shard_map(body, mesh=mesh, in_specs=(spec,) * 5, out_specs=(spec,) * 5, check_vma=False)
```

```python
import math

import jax
import jax.numpy as jnp
from jax import lax
from jax.experimental import pallas as pl
from jax.experimental.pallas import tpu as pltpu
from jax.sharding import PartitionSpec as P

AXES = ("ctx", "ch")
F32 = jnp.float32
BF16 = jnp.bfloat16


def build_tables(first, second):
    points = first * second
    half = first // 2
    rows_first = jnp.arange(first, dtype=jnp.int32)
    rows_half = jnp.arange(half, dtype=jnp.int32)
    rows_second = jnp.arange(second, dtype=jnp.int32)
    outer_phase = rows_first[:, None] * rows_half[None, :] % first
    outer_angle = outer_phase.astype(F32) * (2.0 * math.pi / first)
    turn_phase = rows_first[:, None] * rows_second[None, :] % points
    turn_angle = turn_phase.astype(F32) * (2.0 * math.pi / points)
    inner_phase = rows_second[:, None] * rows_second[None, :] % second
    inner_angle = inner_phase.astype(F32) * (2.0 * math.pi / second)
    return (
        jnp.cos(outer_angle).astype(BF16),
        jnp.sin(outer_angle).astype(BF16),
        jnp.cos(turn_angle),
        jnp.sin(turn_angle),
        jnp.cos(inner_angle).astype(BF16),
        jnp.sin(inner_angle).astype(BF16),
    )


def mm(spec, left, right):
    return jnp.einsum(spec, left.astype(BF16), right.astype(BF16), preferred_element_type=F32)


def forward_spectrum(tables, signal):
    outer_cos, outer_sin, turn_cos, turn_sin, inner_cos, inner_sin = tables
    half = outer_cos.shape[1]
    second = inner_cos.shape[0]
    shaped = signal.reshape(signal.shape[0], half, second)
    real_outer = mm("kn,cnm->ckm", outer_cos, shaped)
    imag_outer = -mm("kn,cnm->ckm", outer_sin, shaped)
    real_turned = real_outer * turn_cos + imag_outer * turn_sin
    imag_turned = imag_outer * turn_cos - real_outer * turn_sin
    real_spec = mm("ckn,mn->ckm", real_turned, inner_cos) + mm("ckn,mn->ckm", imag_turned, inner_sin)
    imag_spec = mm("ckn,mn->ckm", imag_turned, inner_cos) - mm("ckn,mn->ckm", real_turned, inner_sin)
    return (real_spec, imag_spec)


def inverse_signal(tables, spec_pair, scale):
    outer_cos, outer_sin, turn_cos, turn_sin, inner_cos, inner_sin = tables
    real_spec, imag_spec = spec_pair
    real_inner = mm("ckn,mn->ckm", real_spec, inner_cos) - mm("ckn,mn->ckm", imag_spec, inner_sin)
    imag_inner = mm("ckn,mn->ckm", imag_spec, inner_cos) + mm("ckn,mn->ckm", real_spec, inner_sin)
    real_turned = (real_inner * turn_cos - imag_inner * turn_sin) * scale
    imag_turned = (imag_inner * turn_cos + real_inner * turn_sin) * scale
    result = mm("kn,ckm->cnm", outer_cos, real_turned) - mm("kn,ckm->cnm", outer_sin, imag_turned)
    return result.reshape(result.shape[0], -1)


def product(left_pair, right_pair):
    return (
        left_pair[0] * right_pair[0] - left_pair[1] * right_pair[1],
        left_pair[0] * right_pair[1] + left_pair[1] * right_pair[0],
    )


def product_conj(left_pair, right_pair):
    return (
        left_pair[0] * right_pair[0] + left_pair[1] * right_pair[1],
        left_pair[1] * right_pair[0] - left_pair[0] * right_pair[1],
    )


def to_channels(arrays):
    rows, width = arrays[0].shape
    devices = lax.psum(1, AXES)
    per_device = width // devices
    packed = jnp.concatenate([a.T.reshape(devices, per_device, rows) for a in arrays], axis=1)
    moved = lax.all_to_all(packed, AXES, split_axis=0, concat_axis=0, tiled=True)
    moved = moved.reshape(devices, len(arrays), per_device, rows).transpose(1, 2, 0, 3)
    return moved.reshape(len(arrays), per_device, devices * rows)


def to_tokens(cols):
    count, per_device, length = cols.shape
    devices = lax.psum(1, AXES)
    rows = length // devices
    packed = cols.reshape(count, per_device, devices, rows).transpose(2, 0, 1, 3)
    moved = lax.all_to_all(packed.reshape(devices, count * per_device, rows), AXES, split_axis=0, concat_axis=0, tiled=True)
    moved = moved.reshape(devices, count, per_device, rows).transpose(1, 3, 0, 2)
    return moved.reshape(count, rows, devices * per_device)


def kernel_tables(first, second, rows):
    outer_cos, outer_sin, turn_cos, turn_sin, inner_cos, inner_sin = build_tables(first, second)
    stage_one = jnp.concatenate([outer_cos[:rows], -outer_sin[:rows]], axis=0)
    forward_two = jnp.concatenate(
        [jnp.concatenate([inner_cos, -inner_sin], axis=1), jnp.concatenate([inner_sin, inner_cos], axis=1)], axis=0
    )
    inverse_two = jnp.concatenate(
        [jnp.concatenate([inner_cos, inner_sin], axis=1), jnp.concatenate([-inner_sin, inner_cos], axis=1)], axis=0
    )
    index = jnp.arange(rows)
    weight = jnp.where((index == 0) | (index == first // 2), 1.0, jnp.where(index < first // 2, 2.0, 0.0))
    weight = weight.astype(F32)[None, :]
    stage_last = jnp.concatenate(
        [outer_cos[:rows].T.astype(F32) * weight, -outer_sin[:rows].T.astype(F32) * weight], axis=1
    )
    return (stage_one, turn_cos[:rows], turn_sin[:rows], forward_two, inverse_two, stage_last)


def conv_kernel(block, sig_ref, one_ref, tc_ref, ts_ref, two_ref, inv_ref, last_ref, out_ref, turned_ref, spec_ref):
    first = tc_ref.shape[0]
    second = tc_ref.shape[1]

    def dot(left, right):
        return jnp.dot(left, right, preferred_element_type=F32)

    def rows_of(signal, c):
        return pl.ds(pl.multiple_of((signal * block + c) * first, first), first)

    def stage_one(c, carry):
        for signal in range(3):
            source = sig_ref.at[signal]
            outer = dot(one_ref[...], source[c])
            real, imag = outer[:first], outer[first:]
            turn_c, turn_s = tc_ref[...], ts_ref[...]
            turned = jnp.concatenate([real * turn_c + imag * turn_s, imag * turn_c - real * turn_s], axis=1)
            turned_ref[rows_of(signal, c), :] = turned.astype(BF16)
        return carry

    lax.fori_loop(0, block, stage_one, 0)
    spec_ref[...] = dot(turned_ref[...], two_ref[...])

    def products(c, carry):
        g = spec_ref[rows_of(0, c), :]
        t = spec_ref[rows_of(1, c), :]
        b = spec_ref[rows_of(2, c), :]
        g_re, g_im = g[:, :second], g[:, second:]
        t_re, t_im = t[:, :second], t[:, second:]
        b_re, b_im = b[:, :second], b[:, second:]
        pairs = (
            (t_re * g_re - t_im * g_im, t_re * g_im + t_im * g_re),
            (b_re * t_re + b_im * t_im, b_im * t_re - b_re * t_im),
            (b_re * g_re + b_im * g_im, b_im * g_re - b_re * g_im),
        )
        for j, (real, imag) in enumerate(pairs):
            turned_ref[rows_of(j, c), :] = jnp.concatenate([real, imag], axis=1).astype(BF16)
        return carry

    lax.fori_loop(0, block, products, 0)
    spec_ref[...] = dot(turned_ref[...], inv_ref[...])

    def stage_last(c, carry):
        turn_c, turn_s = tc_ref[...], ts_ref[...]
        for j in range(3):
            inner = spec_ref[rows_of(j, c), :]
            inner_re, inner_im = inner[:, :second], inner[:, second:]
            turned = jnp.concatenate(
                [inner_re * turn_c - inner_im * turn_s, inner_im * turn_c + inner_re * turn_s], axis=0
            )
            out_ref[j, c] = dot(last_ref[...], turned.astype(BF16)).astype(out_ref.dtype)
        return carry

    lax.fori_loop(0, block, stage_last, 0)


def convolve(signals, block=8, rows=None):
    _, channels, length = signals.shape
    points = 2 * length
    second = math.gcd(points, 128)
    first = points // second
    half = first // 2
    scale = 1.0 / (math.sqrt(length) * points)
    if rows is None:
        rows = min(first, -(-(half + 1) // 16) * 16)
    stage_one, turn_c, turn_s, forward_two, inverse_two, stage_last = kernel_tables(first, second, rows)
    tables = (stage_one, turn_c, turn_s, forward_two, inverse_two, (stage_last.astype(F32) * scale).astype(BF16))
    shaped = signals.reshape(3, channels, half, second)

    def whole(shape):
        return pl.BlockSpec(shape, lambda i: (0,) * len(shape))

    out = pl.pallas_call(
        lambda *refs: conv_kernel(block, *refs),
        grid=(channels // block,),
        in_specs=[
            pl.BlockSpec((3, block, half, second), lambda i: (0, i, 0, 0)),
        ]
        + [whole(t.shape) for t in tables],
        out_specs=pl.BlockSpec((3, block, half, second), lambda i: (0, i, 0, 0)),
        out_shape=jax.ShapeDtypeStruct((3, channels, half, second), BF16),
        scratch_shapes=[pltpu.VMEM((3 * block * rows, 2 * second), BF16), pltpu.VMEM((3 * block * rows, 2 * second), F32)],
        compiler_params=pltpu.CompilerParams(dimension_semantics=("arbitrary",)),
        name="hyena_conv",
    )(shaped, *tables)
    return out.reshape(3, channels, length)


def pack_kernel(key_ref, value_ref, taps_ref, grad_ref, query_ref, out_ref):
    block_devices, total, rows = out_ref.shape
    per = total // 3
    gated = key_ref[...].astype(F32) * value_ref[...].astype(F32)
    back_in = grad_ref[...].astype(F32) * query_ref[...].astype(F32)
    for a, values in enumerate((gated, taps_ref[...].astype(F32), back_in)):
        out_ref[:, a * per:(a + 1) * per, :] = values.T.astype(BF16).reshape(block_devices, per, rows)


def pack(chunk, chunks, key, value, taps, grad, query, steps=4):
    rows, width = key.shape
    devices = lax.psum(1, AXES)
    per = width // (chunks * devices)
    cols = width // (chunks * steps)
    in_spec = pl.BlockSpec((rows, cols), lambda i: (0, chunk * steps + i))
    return pl.pallas_call(
        pack_kernel,
        grid=(steps,),
        in_specs=[in_spec] * 5,
        out_specs=pl.BlockSpec((devices // steps, 3 * per, rows), lambda i: (i, 0, 0)),
        out_shape=jax.ShapeDtypeStruct((devices, 3 * per, rows), BF16),
        compiler_params=pltpu.CompilerParams(dimension_semantics=("arbitrary",)),
        name="hyena_pack",
    )(key, value, taps, grad, query)


def unpack_kernel(moved_ref, query_ref, grad_ref, key_ref, value_ref, *refs):
    mixed_ref, q_grad_ref, k_grad_ref, v_grad_ref, filter_ref = refs[-5:]
    block_devices, total, rows = moved_ref.shape
    per = total // 3

    def part(a):
        return moved_ref[:, a * per:(a + 1) * per, :].reshape(block_devices * per, rows).astype(F32).T

    conv_back = part(0)
    mixed_ref[...] = (query_ref[...].astype(F32) * conv_back).astype(BF16)
    q_grad_ref[...] = (grad_ref[...].astype(F32) * conv_back).astype(BF16)
    grad_back = part(1)
    k_grad_ref[...] = (grad_back * value_ref[...].astype(F32)).astype(BF16)
    v_grad_ref[...] = (grad_back * key_ref[...].astype(F32)).astype(BF16)
    filter_ref[...] = part(2).astype(BF16)


def unpack(chunk, chunks, moved, query, grad, key, value, previous=None, steps=4):
    rows, width = key.shape
    devices = moved.shape[0]
    cols = width // (chunks * steps)
    spec = pl.BlockSpec((rows, cols), lambda i: (0, chunk * steps + i))
    in_specs = [pl.BlockSpec((devices // steps, moved.shape[1], rows), lambda i: (i, 0, 0))] + [spec] * 4
    operands = [moved, query, grad, key, value]
    aliases = {}
    if previous is not None:
        in_specs += [pl.BlockSpec(memory_space=pl.ANY)] * 5
        aliases = {5 + j: j for j in range(5)}
        operands += list(previous)
    return pl.pallas_call(
        unpack_kernel,
        grid=(steps,),
        in_specs=in_specs,
        out_specs=[spec] * 5,
        out_shape=[jax.ShapeDtypeStruct((rows, width), BF16)] * 5,
        input_output_aliases=aliases,
        compiler_params=pltpu.CompilerParams(dimension_semantics=("arbitrary",)),
        name="hyena_unpack",
    )(*operands)


def from_packed(moved, count):
    devices, total, rows = moved.shape
    per = total // count
    return moved.reshape(devices, count, per, rows).transpose(1, 2, 0, 3).reshape(count, per, devices * rows)


def to_packed(cols):
    count, per, length = cols.shape
    devices = lax.psum(1, AXES)
    rows = length // devices
    return cols.reshape(count, per, devices, rows).transpose(2, 0, 1, 3).reshape(devices, count * per, rows)


def body(q_proj, k_proj, v_proj, filter_taps, out_grad, chunks=2):
    outputs = None
    packed = [pack(h, chunks, k_proj, v_proj, filter_taps, out_grad, q_proj) for h in range(chunks)]
    for h in range(chunks):
        arrived = lax.all_to_all(packed[h], AXES, split_axis=0, concat_axis=0, tiled=True)
        results = convolve(from_packed(arrived, 3))
        back = lax.all_to_all(to_packed(results), AXES, split_axis=0, concat_axis=0, tiled=True)
        outputs = unpack(h, chunks, back, q_proj, out_grad, k_proj, v_proj, outputs)
    return tuple(outputs)


def solution(mesh):
    spec = P(AXES, None)
    return jax.shard_map(body, mesh=mesh, in_specs=(spec,) * 5, out_specs=(spec,) * 5, check_vma=False)
```

```python
import math

import jax
import numpy as np
import jax.numpy as jnp
from jax import lax
from jax.experimental import pallas as pl
from jax.experimental.pallas import tpu as pltpu
from jax.sharding import PartitionSpec as P

AXES = ("ctx", "ch")
F32 = jnp.float32
BF16 = jnp.bfloat16


def build_tables(first, second):
    points = first * second
    half = first // 2
    rows_first = np.arange(first)
    rows_half = np.arange(half)
    rows_second = np.arange(second)
    outer_angle = (rows_first[:, None] * rows_half[None, :] % first) * (2.0 * math.pi / first)
    turn_angle = (rows_first[:, None] * rows_second[None, :] % points) * (2.0 * math.pi / points)
    inner_angle = (rows_second[:, None] * rows_second[None, :] % second) * (2.0 * math.pi / second)
    return (
        np.cos(outer_angle),
        np.sin(outer_angle),
        np.cos(turn_angle),
        np.sin(turn_angle),
        np.cos(inner_angle),
        np.sin(inner_angle),
    )


def kernel_tables(first, second, rows, scale):
    outer_cos, outer_sin, turn_cos, turn_sin, inner_cos, inner_sin = build_tables(first, second)
    stage_one = np.concatenate([outer_cos[:rows], -outer_sin[:rows]], axis=0)
    forward_two = np.block([[inner_cos, -inner_sin], [inner_sin, inner_cos]])
    inverse_two = np.block([[inner_cos, inner_sin], [-inner_sin, inner_cos]])
    index = np.arange(rows)
    weight = np.where((index == 0) | (index == first // 2), 1.0, np.where(index < first // 2, 2.0, 0.0))[None, :]
    stage_last = np.concatenate([outer_cos[:rows].T * weight, -outer_sin[:rows].T * weight], axis=1) * scale
    return (
        jnp.asarray(stage_one.astype(BF16)),
        jnp.asarray(turn_cos[:rows].astype(np.float32)),
        jnp.asarray(turn_sin[:rows].astype(np.float32)),
        jnp.asarray(forward_two.astype(BF16)),
        jnp.asarray(inverse_two.astype(BF16)),
        jnp.asarray(stage_last.astype(BF16)),
    )


def conv_kernel(block, sig_ref, one_ref, tc_ref, ts_ref, two_ref, inv_ref, last_ref, out_ref, turned_ref, spec_ref):
    first = tc_ref.shape[0]
    second = tc_ref.shape[1]

    def dot(left, right):
        return jnp.dot(left, right, preferred_element_type=F32)

    def rows_of(signal, c):
        return pl.ds(pl.multiple_of((signal * block + c) * first, first), first)

    def stage_one(c, carry):
        for signal in range(3):
            source = sig_ref.at[signal]
            outer = dot(one_ref[...], source[c])
            real, imag = outer[:first], outer[first:]
            turn_c, turn_s = tc_ref[...], ts_ref[...]
            turned = jnp.concatenate([real * turn_c + imag * turn_s, imag * turn_c - real * turn_s], axis=1)
            turned_ref[rows_of(signal, c), :] = turned.astype(BF16)
        return carry

    lax.fori_loop(0, block, stage_one, 0)
    spec_ref[...] = dot(turned_ref[...], two_ref[...])

    def products(c, carry):
        g = spec_ref[rows_of(0, c), :]
        t = spec_ref[rows_of(1, c), :]
        b = spec_ref[rows_of(2, c), :]
        g_re, g_im = g[:, :second], g[:, second:]
        t_re, t_im = t[:, :second], t[:, second:]
        b_re, b_im = b[:, :second], b[:, second:]
        pairs = (
            (t_re * g_re - t_im * g_im, t_re * g_im + t_im * g_re),
            (b_re * t_re + b_im * t_im, b_im * t_re - b_re * t_im),
            (b_re * g_re + b_im * g_im, b_im * g_re - b_re * g_im),
        )
        for j, (real, imag) in enumerate(pairs):
            turned_ref[rows_of(j, c), :] = jnp.concatenate([real, imag], axis=1).astype(BF16)
        return carry

    lax.fori_loop(0, block, products, 0)
    spec_ref[...] = dot(turned_ref[...], inv_ref[...])

    def stage_last(c, carry):
        turn_c, turn_s = tc_ref[...], ts_ref[...]
        for j in range(3):
            inner = spec_ref[rows_of(j, c), :]
            inner_re, inner_im = inner[:, :second], inner[:, second:]
            turned = jnp.concatenate(
                [inner_re * turn_c - inner_im * turn_s, inner_im * turn_c + inner_re * turn_s], axis=0
            )
            out_ref[j, c] = dot(last_ref[...], turned.astype(BF16)).astype(out_ref.dtype)
        return carry

    lax.fori_loop(0, block, stage_last, 0)


def convolve(signals, block=8, rows=None):
    _, channels, length = signals.shape
    points = 2 * length
    second = math.gcd(points, 128)
    first = points // second
    half = first // 2
    scale = 1.0 / (math.sqrt(length) * points)
    if rows is None:
        rows = min(first, -(-(half + 1) // 16) * 16)
    tables = kernel_tables(first, second, rows, scale)
    shaped = signals.reshape(3, channels, half, second)

    def whole(shape):
        return pl.BlockSpec(shape, lambda i: (0,) * len(shape))

    out = pl.pallas_call(
        lambda *refs: conv_kernel(block, *refs),
        grid=(channels // block,),
        in_specs=[
            pl.BlockSpec((3, block, half, second), lambda i: (0, i, 0, 0)),
        ]
        + [whole(t.shape) for t in tables],
        out_specs=pl.BlockSpec((3, block, half, second), lambda i: (0, i, 0, 0)),
        out_shape=jax.ShapeDtypeStruct((3, channels, half, second), BF16),
        scratch_shapes=[pltpu.VMEM((3 * block * rows, 2 * second), BF16), pltpu.VMEM((3 * block * rows, 2 * second), F32)],
        compiler_params=pltpu.CompilerParams(dimension_semantics=("arbitrary",)),
        name="hyena_conv",
    )(shaped, *tables)
    return out.reshape(3, channels, length)


def pack_kernel(key_ref, value_ref, taps_ref, grad_ref, query_ref, out_ref):
    block_devices, total, rows = out_ref.shape
    per = total // 3
    gated = key_ref[...].astype(F32) * value_ref[...].astype(F32)
    back_in = grad_ref[...].astype(F32) * query_ref[...].astype(F32)
    for a, values in enumerate((gated, taps_ref[...].astype(F32), back_in)):
        out_ref[:, a * per:(a + 1) * per, :] = values.T.astype(BF16).reshape(block_devices, per, rows)


def pack(chunk, chunks, key, value, taps, grad, query, steps=4):
    rows, width = key.shape
    devices = lax.psum(1, AXES)
    per = width // (chunks * devices)
    cols = width // (chunks * steps)
    in_spec = pl.BlockSpec((rows, cols), lambda i: (0, chunk * steps + i))
    return pl.pallas_call(
        pack_kernel,
        grid=(steps,),
        in_specs=[in_spec] * 5,
        out_specs=pl.BlockSpec((devices // steps, 3 * per, rows), lambda i: (i, 0, 0)),
        out_shape=jax.ShapeDtypeStruct((devices, 3 * per, rows), BF16),
        compiler_params=pltpu.CompilerParams(dimension_semantics=("arbitrary",)),
        name="hyena_pack",
    )(key, value, taps, grad, query)


def unpack_kernel(moved_ref, query_ref, grad_ref, key_ref, value_ref, *refs):
    mixed_ref, q_grad_ref, k_grad_ref, v_grad_ref, filter_ref = refs[-5:]
    block_devices, total, rows = moved_ref.shape
    per = total // 3

    def part(a):
        return moved_ref[:, a * per:(a + 1) * per, :].reshape(block_devices * per, rows).astype(F32).T

    conv_back = part(0)
    mixed_ref[...] = (query_ref[...].astype(F32) * conv_back).astype(BF16)
    q_grad_ref[...] = (grad_ref[...].astype(F32) * conv_back).astype(BF16)
    grad_back = part(1)
    k_grad_ref[...] = (grad_back * value_ref[...].astype(F32)).astype(BF16)
    v_grad_ref[...] = (grad_back * key_ref[...].astype(F32)).astype(BF16)
    filter_ref[...] = part(2).astype(BF16)


def unpack(chunk, chunks, moved, query, grad, key, value, previous=None, steps=4):
    rows, width = key.shape
    devices = moved.shape[0]
    cols = width // (chunks * steps)
    spec = pl.BlockSpec((rows, cols), lambda i: (0, chunk * steps + i))
    in_specs = [pl.BlockSpec((devices // steps, moved.shape[1], rows), lambda i: (i, 0, 0))] + [spec] * 4
    operands = [moved, query, grad, key, value]
    aliases = {}
    if previous is not None:
        in_specs += [pl.BlockSpec(memory_space=pl.ANY)] * 5
        aliases = {5 + j: j for j in range(5)}
        operands += list(previous)
    return pl.pallas_call(
        unpack_kernel,
        grid=(steps,),
        in_specs=in_specs,
        out_specs=[spec] * 5,
        out_shape=[jax.ShapeDtypeStruct((rows, width), BF16)] * 5,
        input_output_aliases=aliases,
        compiler_params=pltpu.CompilerParams(dimension_semantics=("arbitrary",)),
        name="hyena_unpack",
    )(*operands)


def from_packed(moved, count):
    devices, total, rows = moved.shape
    per = total // count
    return moved.reshape(devices, count, per, rows).transpose(1, 2, 0, 3).reshape(count, per, devices * rows)


def to_packed(cols):
    count, per, length = cols.shape
    devices = lax.psum(1, AXES)
    rows = length // devices
    return cols.reshape(count, per, devices, rows).transpose(2, 0, 1, 3).reshape(devices, count * per, rows)


def body(q_proj, k_proj, v_proj, filter_taps, out_grad, chunks=2):
    outputs = None
    packed = [pack(h, chunks, k_proj, v_proj, filter_taps, out_grad, q_proj) for h in range(chunks)]
    for h in range(chunks):
        arrived = lax.all_to_all(packed[h], AXES, split_axis=0, concat_axis=0, tiled=True)
        results = convolve(from_packed(arrived, 3))
        back = lax.all_to_all(to_packed(results), AXES, split_axis=0, concat_axis=0, tiled=True)
        outputs = unpack(h, chunks, back, q_proj, out_grad, k_proj, v_proj, outputs)
    return tuple(outputs)


def solution(mesh):
    spec = P(AXES, None)
    return jax.shard_map(body, mesh=mesh, in_specs=(spec,) * 5, out_specs=(spec,) * 5, check_vma=False)
```

```python
import math

import jax
import numpy as np
import jax.numpy as jnp
from jax import lax
from jax.experimental import pallas as pl
from jax.experimental.pallas import tpu as pltpu
from jax.sharding import PartitionSpec as P

AXES = ("ctx", "ch")
F32 = jnp.float32
BF16 = jnp.bfloat16


def build_tables(first, second):
    points = first * second
    half = first // 2
    rows_first = np.arange(first)
    rows_half = np.arange(half)
    rows_second = np.arange(second)
    outer_angle = (rows_first[:, None] * rows_half[None, :] % first) * (2.0 * math.pi / first)
    turn_angle = (rows_first[:, None] * rows_second[None, :] % points) * (2.0 * math.pi / points)
    inner_angle = (rows_second[:, None] * rows_second[None, :] % second) * (2.0 * math.pi / second)
    return (
        np.cos(outer_angle),
        np.sin(outer_angle),
        np.cos(turn_angle),
        np.sin(turn_angle),
        np.cos(inner_angle),
        np.sin(inner_angle),
    )


def kernel_tables(first, second, rows, scale):
    outer_cos, outer_sin, turn_cos, turn_sin, inner_cos, inner_sin = build_tables(first, second)
    stage_one = np.concatenate([outer_cos[:rows], -outer_sin[:rows]], axis=0)
    forward_two = np.block([[inner_cos, -inner_sin], [inner_sin, inner_cos]])
    inverse_two = np.block([[inner_cos, inner_sin], [-inner_sin, inner_cos]])
    index = np.arange(rows)
    weight = np.where((index == 0) | (index == first // 2), 1.0, np.where(index < first // 2, 2.0, 0.0))[None, :]
    stage_last = np.concatenate([outer_cos[:rows].T * weight, -outer_sin[:rows].T * weight], axis=1) * scale
    return (
        jnp.asarray(stage_one.astype(BF16)),
        jnp.asarray(turn_cos[:rows].astype(np.float32)),
        jnp.asarray(turn_sin[:rows].astype(np.float32)),
        jnp.asarray(forward_two.astype(BF16)),
        jnp.asarray(inverse_two.astype(BF16)),
        jnp.asarray(stage_last.astype(BF16)),
    )


def conv_kernel(block, sig_ref, one_ref, tc_ref, ts_ref, two_ref, inv_ref, last_ref, out_ref, turned_ref, spec_ref):
    first = tc_ref.shape[0]
    second = tc_ref.shape[1]

    def dot(left, right):
        return jnp.dot(left, right, preferred_element_type=F32)

    def rows_of(signal, c):
        return pl.ds(pl.multiple_of((signal * block + c) * first, first), first)

    def stage_one(c, carry):
        for signal in range(3):
            source = sig_ref.at[signal]
            outer = dot(one_ref[...], source[c])
            real, imag = outer[:first], outer[first:]
            turn_c, turn_s = tc_ref[...], ts_ref[...]
            turned = jnp.concatenate([real * turn_c + imag * turn_s, imag * turn_c - real * turn_s], axis=1)
            turned_ref[rows_of(signal, c), :] = turned.astype(BF16)
        return carry

    lax.fori_loop(0, block, stage_one, 0)
    spec_ref[...] = dot(turned_ref[...], two_ref[...])

    def products(c, carry):
        g = spec_ref[rows_of(0, c), :]
        t = spec_ref[rows_of(1, c), :]
        b = spec_ref[rows_of(2, c), :]
        g_re, g_im = g[:, :second], g[:, second:]
        t_re, t_im = t[:, :second], t[:, second:]
        b_re, b_im = b[:, :second], b[:, second:]
        pairs = (
            (t_re * g_re - t_im * g_im, t_re * g_im + t_im * g_re),
            (b_re * t_re + b_im * t_im, b_im * t_re - b_re * t_im),
            (b_re * g_re + b_im * g_im, b_im * g_re - b_re * g_im),
        )
        for j, (real, imag) in enumerate(pairs):
            turned_ref[rows_of(j, c), :] = jnp.concatenate([real, imag], axis=1).astype(BF16)
        return carry

    lax.fori_loop(0, block, products, 0)
    spec_ref[...] = dot(turned_ref[...], inv_ref[...])

    def stage_last(c, carry):
        turn_c, turn_s = tc_ref[...], ts_ref[...]
        for j in range(3):
            inner = spec_ref[rows_of(j, c), :]
            inner_re, inner_im = inner[:, :second], inner[:, second:]
            turned = jnp.concatenate(
                [inner_re * turn_c - inner_im * turn_s, inner_im * turn_c + inner_re * turn_s], axis=0
            )
            out_ref[j, c] = dot(last_ref[...], turned.astype(BF16)).astype(out_ref.dtype)
        return carry

    lax.fori_loop(0, block, stage_last, 0)


def convolve(signals, block=8, rows=None):
    _, channels, length = signals.shape
    points = 2 * length
    second = math.gcd(points, 128)
    first = points // second
    half = first // 2
    scale = 1.0 / (math.sqrt(length) * points)
    if rows is None:
        rows = min(first, -(-(half + 1) // 16) * 16)
    tables = kernel_tables(first, second, rows, scale)
    shaped = signals.reshape(3, channels, half, second)

    def whole(shape):
        return pl.BlockSpec(shape, lambda i: (0,) * len(shape))

    out = pl.pallas_call(
        lambda *refs: conv_kernel(block, *refs),
        grid=(channels // block,),
        in_specs=[
            pl.BlockSpec((3, block, half, second), lambda i: (0, i, 0, 0)),
        ]
        + [whole(t.shape) for t in tables],
        out_specs=pl.BlockSpec((3, block, half, second), lambda i: (0, i, 0, 0)),
        out_shape=jax.ShapeDtypeStruct((3, channels, half, second), BF16),
        scratch_shapes=[pltpu.VMEM((3 * block * rows, 2 * second), BF16), pltpu.VMEM((3 * block * rows, 2 * second), F32)],
        compiler_params=pltpu.CompilerParams(dimension_semantics=("arbitrary",)),
        name="hyena_conv",
    )(shaped, *tables)
    return out.reshape(3, channels, length)


def pack_kernel(key_ref, value_ref, taps_ref, grad_ref, query_ref, out_ref):
    block_devices, total, rows = out_ref.shape
    per = total // 3
    gated = key_ref[...].astype(F32) * value_ref[...].astype(F32)
    back_in = grad_ref[...].astype(F32) * query_ref[...].astype(F32)
    for a, values in enumerate((gated, taps_ref[...].astype(F32), back_in)):
        out_ref[:, a * per:(a + 1) * per, :] = values.T.astype(BF16).reshape(block_devices, per, rows)


def pack(chunk, chunks, key, value, taps, grad, query, steps=2):
    rows, width = key.shape
    devices = lax.psum(1, AXES)
    per = width // (chunks * devices)
    cols = width // (chunks * steps)
    in_spec = pl.BlockSpec((rows, cols), lambda i: (0, chunk * steps + i))
    return pl.pallas_call(
        pack_kernel,
        grid=(steps,),
        in_specs=[in_spec] * 5,
        out_specs=pl.BlockSpec((devices // steps, 3 * per, rows), lambda i: (i, 0, 0)),
        out_shape=jax.ShapeDtypeStruct((devices, 3 * per, rows), BF16),
        compiler_params=pltpu.CompilerParams(dimension_semantics=("arbitrary",)),
        name="hyena_pack",
    )(key, value, taps, grad, query)


def unpack_kernel(moved_ref, query_ref, grad_ref, key_ref, value_ref, *refs):
    mixed_ref, q_grad_ref, k_grad_ref, v_grad_ref, filter_ref = refs[-5:]
    block_devices, total, rows = moved_ref.shape
    per = total // 3

    def part(a):
        return moved_ref[:, a * per:(a + 1) * per, :].reshape(block_devices * per, rows).astype(F32).T

    conv_back = part(0)
    mixed_ref[...] = (query_ref[...].astype(F32) * conv_back).astype(BF16)
    q_grad_ref[...] = (grad_ref[...].astype(F32) * conv_back).astype(BF16)
    grad_back = part(1)
    k_grad_ref[...] = (grad_back * value_ref[...].astype(F32)).astype(BF16)
    v_grad_ref[...] = (grad_back * key_ref[...].astype(F32)).astype(BF16)
    filter_ref[...] = part(2).astype(BF16)


def unpack(chunk, chunks, moved, query, grad, key, value, previous=None, steps=2):
    rows, width = key.shape
    devices = moved.shape[0]
    cols = width // (chunks * steps)
    spec = pl.BlockSpec((rows, cols), lambda i: (0, chunk * steps + i))
    in_specs = [pl.BlockSpec((devices // steps, moved.shape[1], rows), lambda i: (i, 0, 0))] + [spec] * 4
    operands = [moved, query, grad, key, value]
    aliases = {}
    if previous is not None:
        in_specs += [pl.BlockSpec(memory_space=pl.ANY)] * 5
        aliases = {5 + j: j for j in range(5)}
        operands += list(previous)
    return pl.pallas_call(
        unpack_kernel,
        grid=(steps,),
        in_specs=in_specs,
        out_specs=[spec] * 5,
        out_shape=[jax.ShapeDtypeStruct((rows, width), BF16)] * 5,
        input_output_aliases=aliases,
        compiler_params=pltpu.CompilerParams(dimension_semantics=("arbitrary",)),
        name="hyena_unpack",
    )(*operands)


def from_packed(moved, count):
    devices, total, rows = moved.shape
    per = total // count
    return moved.reshape(devices, count, per, rows).transpose(1, 2, 0, 3).reshape(count, per, devices * rows)


def to_packed(cols):
    count, per, length = cols.shape
    devices = lax.psum(1, AXES)
    rows = length // devices
    return cols.reshape(count, per, devices, rows).transpose(2, 0, 1, 3).reshape(devices, count * per, rows)


def body(q_proj, k_proj, v_proj, filter_taps, out_grad, chunks=2):
    outputs = None
    packed = [pack(h, chunks, k_proj, v_proj, filter_taps, out_grad, q_proj) for h in range(chunks)]
    for h in range(chunks):
        arrived = lax.all_to_all(packed[h], AXES, split_axis=0, concat_axis=0, tiled=True)
        results = convolve(from_packed(arrived, 3))
        back = lax.all_to_all(to_packed(results), AXES, split_axis=0, concat_axis=0, tiled=True)
        outputs = unpack(h, chunks, back, q_proj, out_grad, k_proj, v_proj, outputs)
    return tuple(outputs)


def solution(mesh):
    spec = P(AXES, None)
    return jax.shard_map(body, mesh=mesh, in_specs=(spec,) * 5, out_specs=(spec,) * 5, check_vma=False)
```

```python
import math

import jax
import numpy as np
import jax.numpy as jnp
from jax import lax
from jax.experimental import pallas as pl
from jax.experimental.pallas import tpu as pltpu
from jax.sharding import PartitionSpec as P

AXES = ("ctx", "ch")
F32 = jnp.float32
BF16 = jnp.bfloat16


def build_tables(first, second):
    points = first * second
    half = first // 2
    rows_first = np.arange(first)
    rows_half = np.arange(half)
    rows_second = np.arange(second)
    outer_angle = (rows_first[:, None] * rows_half[None, :] % first) * (2.0 * math.pi / first)
    turn_angle = (rows_first[:, None] * rows_second[None, :] % points) * (2.0 * math.pi / points)
    inner_angle = (rows_second[:, None] * rows_second[None, :] % second) * (2.0 * math.pi / second)
    return (
        np.cos(outer_angle),
        np.sin(outer_angle),
        np.cos(turn_angle),
        np.sin(turn_angle),
        np.cos(inner_angle),
        np.sin(inner_angle),
    )


def kernel_tables(first, second, rows, scale):
    outer_cos, outer_sin, turn_cos, turn_sin, inner_cos, inner_sin = build_tables(first, second)
    stage_one = np.concatenate([outer_cos[:rows], -outer_sin[:rows]], axis=0)
    forward_two = np.block([[inner_cos, -inner_sin], [inner_sin, inner_cos]])
    inverse_two = np.block([[inner_cos, inner_sin], [-inner_sin, inner_cos]])
    index = np.arange(rows)
    weight = np.where((index == 0) | (index == first // 2), 1.0, np.where(index < first // 2, 2.0, 0.0))[None, :]
    stage_last = np.concatenate([outer_cos[:rows].T * weight, -outer_sin[:rows].T * weight], axis=1) * scale
    return (
        jnp.asarray(stage_one.astype(BF16)),
        jnp.asarray(turn_cos[:rows].astype(np.float32)),
        jnp.asarray(turn_sin[:rows].astype(np.float32)),
        jnp.asarray(forward_two.astype(BF16)),
        jnp.asarray(inverse_two.astype(BF16)),
        jnp.asarray(stage_last.astype(BF16)),
    )


def conv_kernel(block, sig_ref, one_ref, tc_ref, ts_ref, two_ref, inv_ref, last_ref, out_ref, turned_ref, spec_ref):
    first = tc_ref.shape[0]
    second = tc_ref.shape[1]

    def dot(left, right):
        return jnp.dot(left, right, preferred_element_type=F32)

    def rows_of(signal, c):
        return pl.ds(pl.multiple_of((signal * block + c) * first, first), first)

    def stage_one(c, carry):
        for signal in range(3):
            source = sig_ref.at[signal]
            outer = dot(one_ref[...], source[c])
            real, imag = outer[:first], outer[first:]
            turn_c, turn_s = tc_ref[...], ts_ref[...]
            turned = jnp.concatenate([real * turn_c + imag * turn_s, imag * turn_c - real * turn_s], axis=1)
            turned_ref[rows_of(signal, c), :] = turned.astype(BF16)
        return carry

    lax.fori_loop(0, block, stage_one, 0)
    spec_ref[...] = dot(turned_ref[...], two_ref[...])

    def products(c, carry):
        g = spec_ref[rows_of(0, c), :]
        t = spec_ref[rows_of(1, c), :]
        b = spec_ref[rows_of(2, c), :]
        g_re, g_im = g[:, :second], g[:, second:]
        t_re, t_im = t[:, :second], t[:, second:]
        b_re, b_im = b[:, :second], b[:, second:]
        pairs = (
            (t_re * g_re - t_im * g_im, t_re * g_im + t_im * g_re),
            (b_re * t_re + b_im * t_im, b_im * t_re - b_re * t_im),
            (b_re * g_re + b_im * g_im, b_im * g_re - b_re * g_im),
        )
        for j, (real, imag) in enumerate(pairs):
            turned_ref[rows_of(j, c), :] = jnp.concatenate([real, imag], axis=1).astype(BF16)
        return carry

    lax.fori_loop(0, block, products, 0)
    spec_ref[...] = dot(turned_ref[...], inv_ref[...])

    def stage_last(c, carry):
        turn_c, turn_s = tc_ref[...], ts_ref[...]
        for j in range(3):
            inner = spec_ref[rows_of(j, c), :]
            inner_re, inner_im = inner[:, :second], inner[:, second:]
            turned = jnp.concatenate(
                [inner_re * turn_c - inner_im * turn_s, inner_im * turn_c + inner_re * turn_s], axis=0
            )
            out_ref[j, c] = dot(last_ref[...], turned.astype(BF16)).astype(out_ref.dtype)
        return carry

    lax.fori_loop(0, block, stage_last, 0)


def convolve(signals, block=8, rows=None):
    _, channels, length = signals.shape
    points = 2 * length
    second = math.gcd(points, 128)
    first = points // second
    half = first // 2
    scale = 1.0 / (math.sqrt(length) * points)
    if rows is None:
        rows = min(first, -(-(half + 1) // 16) * 16)
    tables = kernel_tables(first, second, rows, scale)
    shaped = signals.reshape(3, channels, half, second)

    def whole(shape):
        return pl.BlockSpec(shape, lambda i: (0,) * len(shape))

    out = pl.pallas_call(
        lambda *refs: conv_kernel(block, *refs),
        grid=(channels // block,),
        in_specs=[
            pl.BlockSpec((3, block, half, second), lambda i: (0, i, 0, 0)),
        ]
        + [whole(t.shape) for t in tables],
        out_specs=pl.BlockSpec((3, block, half, second), lambda i: (0, i, 0, 0)),
        out_shape=jax.ShapeDtypeStruct((3, channels, half, second), BF16),
        scratch_shapes=[pltpu.VMEM((3 * block * rows, 2 * second), BF16), pltpu.VMEM((3 * block * rows, 2 * second), F32)],
        compiler_params=pltpu.CompilerParams(dimension_semantics=("arbitrary",)),
        name="hyena_conv",
    )(shaped, *tables)
    return out.reshape(3, channels, length)


def pack_kernel(key_ref, value_ref, taps_ref, grad_ref, query_ref, out_ref):
    block_devices, total, rows = out_ref.shape
    per = total // 3
    gated = key_ref[...].astype(F32) * value_ref[...].astype(F32)
    back_in = grad_ref[...].astype(F32) * query_ref[...].astype(F32)
    for a, values in enumerate((gated, taps_ref[...].astype(F32), back_in)):
        out_ref[:, a * per:(a + 1) * per, :] = values.T.astype(BF16).reshape(block_devices, per, rows)


def pack(chunk, chunks, key, value, taps, grad, query, steps=2):
    rows, width = key.shape
    devices = lax.psum(1, AXES)
    per = width // (chunks * devices)
    cols = width // (chunks * steps)
    in_spec = pl.BlockSpec((rows, cols), lambda i: (0, chunk * steps + i))
    return pl.pallas_call(
        pack_kernel,
        grid=(steps,),
        in_specs=[in_spec] * 5,
        out_specs=pl.BlockSpec((devices // steps, 3 * per, rows), lambda i: (i, 0, 0)),
        out_shape=jax.ShapeDtypeStruct((devices, 3 * per, rows), BF16),
        compiler_params=pltpu.CompilerParams(dimension_semantics=("arbitrary",)),
        name="hyena_pack",
    )(key, value, taps, grad, query)


def unpack_kernel(moved_ref, query_ref, grad_ref, key_ref, value_ref, *refs):
    mixed_ref, q_grad_ref, k_grad_ref, v_grad_ref, filter_ref = refs[-5:]
    block_devices, total, rows = moved_ref.shape
    per = total // 3

    def part(a):
        return moved_ref[:, a * per:(a + 1) * per, :].reshape(block_devices * per, rows).astype(F32).T

    conv_back = part(0)
    mixed_ref[...] = (query_ref[...].astype(F32) * conv_back).astype(BF16)
    q_grad_ref[...] = (grad_ref[...].astype(F32) * conv_back).astype(BF16)
    grad_back = part(1)
    k_grad_ref[...] = (grad_back * value_ref[...].astype(F32)).astype(BF16)
    v_grad_ref[...] = (grad_back * key_ref[...].astype(F32)).astype(BF16)
    filter_ref[...] = part(2).astype(BF16)


def unpack(chunk, chunks, moved, query, grad, key, value, previous=None, steps=2):
    rows, width = key.shape
    devices = moved.shape[0]
    cols = width // (chunks * steps)
    spec = pl.BlockSpec((rows, cols), lambda i: (0, chunk * steps + i))
    in_specs = [pl.BlockSpec((devices // steps, moved.shape[1], rows), lambda i: (i, 0, 0))] + [spec] * 4
    operands = [moved, query, grad, key, value]
    aliases = {}
    if previous is not None:
        in_specs += [pl.BlockSpec(memory_space=pl.ANY)] * 5
        aliases = {5 + j: j for j in range(5)}
        operands += list(previous)
    return pl.pallas_call(
        unpack_kernel,
        grid=(steps,),
        in_specs=in_specs,
        out_specs=[spec] * 5,
        out_shape=[jax.ShapeDtypeStruct((rows, width), BF16)] * 5,
        input_output_aliases=aliases,
        compiler_params=pltpu.CompilerParams(dimension_semantics=("arbitrary",)),
        name="hyena_unpack",
    )(*operands)


def from_packed(moved, count):
    devices, total, rows = moved.shape
    per = total // count
    return moved.reshape(devices, count, per, rows).transpose(1, 2, 0, 3).reshape(count, per, devices * rows)


def to_packed(cols):
    count, per, length = cols.shape
    devices = lax.psum(1, AXES)
    rows = length // devices
    return cols.reshape(count, per, devices, rows).transpose(2, 0, 1, 3).reshape(devices, count * per, rows)


def unpack_first(moved, query, grad, key, value):
    devices, total, rows = moved.shape
    per = total // 3
    cols = devices * per
    parts = moved.reshape(devices, 3, per, rows).transpose(1, 3, 0, 2).reshape(3, rows, cols).astype(F32)
    conv_back, grad_back = parts[0], parts[1]
    values = (
        query[:, :cols].astype(F32) * conv_back,
        grad[:, :cols].astype(F32) * conv_back,
        grad_back * value[:, :cols].astype(F32),
        grad_back * key[:, :cols].astype(F32),
        parts[2],
    )
    empty = jnp.zeros(query.shape, BF16)
    return [lax.dynamic_update_slice(empty, v.astype(BF16), (0, 0)) for v in values]


def body(q_proj, k_proj, v_proj, filter_taps, out_grad, chunks=2):
    outputs = None
    packed = [pack(h, chunks, k_proj, v_proj, filter_taps, out_grad, q_proj) for h in range(chunks)]
    for h in range(chunks):
        arrived = lax.all_to_all(packed[h], AXES, split_axis=0, concat_axis=0, tiled=True)
        results = convolve(from_packed(arrived, 3))
        back = lax.all_to_all(to_packed(results), AXES, split_axis=0, concat_axis=0, tiled=True)
        if h == 0:
            outputs = unpack_first(back, q_proj, out_grad, k_proj, v_proj)
        else:
            outputs = unpack(h, chunks, back, q_proj, out_grad, k_proj, v_proj, outputs)
    return tuple(outputs)


def solution(mesh):
    spec = P(AXES, None)
    return jax.shard_map(body, mesh=mesh, in_specs=(spec,) * 5, out_specs=(spec,) * 5, check_vma=False)
```
